256 devices in a mesh: hid: 32 (over z_hi, x, core), wid: 8 (over z_lo, y).
Axes of the slice: x: 4, y: 4, z: 8 (z_hi: 4, z_lo: 2; z = z_hi * 2 + z_lo), core: 2. Of those that a mesh axis runs over, the one named last changes fastest.
Arguments:
- inputs: bfloat16 [768, 8192], P('hid', 'wid'), may hold values from -6 to 6
- gate_weight: bfloat16 [8192, 28672], P('wid', 'hid'), may hold values from -0.0625 to 0.0625
- up_weight: bfloat16 [8192, 28672], P('wid', 'hid'), may hold values from -0.0625 to 0.0625
- down_weight: bfloat16 [28672, 8192], P('hid', 'wid'), may hold values from -0.03125 to 0.03125
- out_grad: bfloat16 [768, 8192], P('hid', 'wid'), may hold values from -0.43164062 to 0.43164062
Outputs:
- input_grad: bfloat16 [768, 8192], P('hid', 'wid')
- gate_grad: bfloat16 [8192, 28672], P('wid', 'hid')
- up_grad: bfloat16 [8192, 28672], P('wid', 'hid')
- down_grad: bfloat16 [28672, 8192], P('hid', 'wid')
The draws below stay inside these ranges and needn't reach their ends.
All inputs are finite; a program needn't handle non-finite values.
Results may differ from the reference program's by a relative error of at most 0.02.
Values may be sent and summed in bfloat16 or wider, within the bound.
No kernel may reach another device: no remote copies, remote signals or barrier semaphores. Data moves between devices by JAX's collectives and lax.ppermute only.
A program may use at most 64 MiB of HBM per device.

```python
import jax
import jax.numpy as jnp
from jax import lax

D = 8192
FF = 28672
TOKENS = 768
DW = 1024
N_WID = 8


def block_levels(own_key, shape, pieces, least, high):
    gain, own = 1.0, jax.random.fold_in(own_key, 6)
    for axis_at, shards_of in pieces:
        heights = jnp.exp(jax.random.uniform(jax.random.fold_in(own, axis_at), (shards_of,), jnp.float32, least / len(pieces), high / len(pieces)))
        gain = gain * jnp.repeat(heights, shape[axis_at] // shards_of).reshape([-1 if axis == axis_at else 1 for axis in range(len(shape))])
    return gain


def bell_draw(rng, extent, width, most, cuts=(), kind=jnp.bfloat16):
    entries = width * jax.random.normal(rng, extent, jnp.float32)
    if cuts:
        entries = entries * block_levels(rng, extent, cuts, -0.22, 0.18)
    return jnp.clip(entries, -most, most).astype(kind)


def setup_inputs(seed: int = 0) -> dict:
    key_list = jax.random.split(jax.random.key(seed), 6)
    return {
        "inputs": bell_draw(key_list[0], (TOKENS, D), 1.0, 6.0, ((0, 32), (1, 8))),
        "gate_weight": bell_draw(key_list[1], (D, FF), D ** -0.5, 0.0625, ((0, 8), (1, 32))),
        "up_weight": bell_draw(key_list[2], (D, FF), D ** -0.5, 0.0625, ((0, 8), (1, 32))),
        "down_weight": bell_draw(key_list[3], (FF, D), FF ** -0.5, 0.03125, ((0, 32), (1, 8))),
        "out_grad": bell_draw(key_list[4], (TOKENS, D), (2.0 / TOKENS ** 0.5), 0.43164062, ((0, 32), (1, 8))),
    }


def rounded(value):
    narrow = lax.optimization_barrier(value.astype(jnp.bfloat16))
    return narrow.astype(jnp.float32)


def blockwise(left, right, contract_right):
    total = jnp.zeros((left.shape[0], right.shape[1 - contract_right]), jnp.float32)
    for block in range(N_WID):
        first = block * DW
        left_cols = left[:, first:first + DW]
        if contract_right == 0:
            part = jnp.dot(left_cols, right[first:first + DW, :], preferred_element_type=jnp.float32)
        else:
            part = lax.dot_general(left_cols, right[:, first:first + DW], (((1,), (1,)), ((), ())), preferred_element_type=jnp.float32)
        total = total + rounded(part)
    return total


def reference(inputs, gate_weight, up_weight, down_weight, out_grad):
    gate = blockwise(inputs, gate_weight, 0)
    up = blockwise(inputs, up_weight, 0)
    hidden_grad = blockwise(out_grad, down_weight, 1)
    sigma = jax.nn.sigmoid(gate)
    hidden = (gate * sigma * up).astype(jnp.bfloat16)
    up_term = (hidden_grad * gate * sigma).astype(jnp.bfloat16)
    gate_term = (hidden_grad * up * sigma * (1.0 + gate * (1.0 - sigma))).astype(jnp.bfloat16)
    contract_last = (((1,), (1,)), ((), ()))
    input_grad = lax.dot_general(gate_term, gate_weight, contract_last, preferred_element_type=jnp.float32)
    input_grad = input_grad + lax.dot_general(up_term, up_weight, contract_last, preferred_element_type=jnp.float32)
    contract_first = (((0,), (0,)), ((), ()))
    gate_grad = lax.dot_general(inputs, gate_term, contract_first, preferred_element_type=jnp.float32).astype(jnp.bfloat16)
    up_grad = lax.dot_general(inputs, up_term, contract_first, preferred_element_type=jnp.float32).astype(jnp.bfloat16)
    down_grad = lax.dot_general(hidden, out_grad, contract_first, preferred_element_type=jnp.float32).astype(jnp.bfloat16)
    return input_grad.astype(jnp.bfloat16), gate_grad, up_grad, down_grad
```

```python
import jax
import jax.numpy as jnp
from jax import lax
from jax.sharding import PartitionSpec as P


def swiglu_terms(gate, up, hidden_grad):
    sigma = jax.nn.sigmoid(gate)
    hidden = (gate * sigma * up).astype(jnp.bfloat16)
    up_term = (hidden_grad * gate * sigma).astype(jnp.bfloat16)
    gate_term = (hidden_grad * up * sigma * (1.0 + gate * (1.0 - sigma))).astype(jnp.bfloat16)
    return (hidden, gate_term, up_term)


def make_per_device(n_hid, n_wid):
    def per_device(inputs, gate_weight, up_weight, down_weight, out_grad):
        dw = inputs.shape[1]
        ff = gate_weight.shape[1]
        both = lax.all_gather(jnp.concatenate([inputs, out_grad], 1), "hid", axis=0, tiled=True)
        all_inputs, all_grads = both[:, :dw], both[:, dw:]
        tokens = all_inputs.shape[0]
        contract_last = (((1,), (1,)), ((), ()))
        gate_part = jnp.dot(all_inputs, gate_weight, preferred_element_type=jnp.float32)
        up_part = jnp.dot(all_inputs, up_weight, preferred_element_type=jnp.float32)
        grad_part = lax.dot_general(
            all_grads, down_weight, contract_last, preferred_element_type=jnp.float32
        )
        parts = jnp.concatenate([gate_part, up_part, grad_part], 1).astype(jnp.bfloat16)
        parts = lax.all_to_all(parts.reshape(n_wid, tokens // n_wid, 3 * ff), "wid", 0, 0, tiled=False)
        sums = jnp.sum(parts.astype(jnp.float32), 0)
        gate, up, hidden_grad = sums[:, :ff], sums[:, ff:2 * ff], sums[:, 2 * ff:]
        terms = jnp.concatenate(swiglu_terms(gate, up, hidden_grad), 1)
        terms = jnp.broadcast_to(terms[None], (n_wid,) + terms.shape)
        terms = lax.all_to_all(terms, "wid", 0, 0, tiled=False).reshape(tokens, 3 * ff)
        hidden, gate_term, up_term = terms[:, :ff], terms[:, ff:2 * ff], terms[:, 2 * ff:]
        total = lax.dot_general(
            gate_term, gate_weight, contract_last, preferred_element_type=jnp.float32
        ) + lax.dot_general(up_term, up_weight, contract_last, preferred_element_type=jnp.float32)
        total = lax.all_to_all(total.reshape(n_hid, tokens // n_hid, dw), "hid", 0, 0, tiled=False)
        input_grad = jnp.sum(total, 0).astype(jnp.bfloat16)
        contract_first = (((0,), (0,)), ((), ()))
        gate_grad = lax.dot_general(
            all_inputs, gate_term, contract_first, preferred_element_type=jnp.float32
        ).astype(jnp.bfloat16)
        up_grad = lax.dot_general(
            all_inputs, up_term, contract_first, preferred_element_type=jnp.float32
        ).astype(jnp.bfloat16)
        down_grad = lax.dot_general(
            hidden, all_grads, contract_first, preferred_element_type=jnp.float32
        ).astype(jnp.bfloat16)
        return (input_grad, gate_grad, up_grad, down_grad)

    return per_device


def solution(mesh):
    placed = (P("hid", "wid"), P("wid", "hid"), P("wid", "hid"), P("hid", "wid"), P("hid", "wid"))
    return jax.shard_map(
        make_per_device(mesh.shape["hid"], mesh.shape["wid"]),
        mesh=mesh,
        in_specs=placed,
        out_specs=(P("hid", "wid"), P("wid", "hid"), P("wid", "hid"), P("hid", "wid")),
        check_vma=False,
    )
```

```python
import jax
import jax.numpy as jnp
from jax import lax
from jax.sharding import Mesh, PartitionSpec as P


def swiglu_terms(gate, up, hidden_grad):
    sigma = jax.nn.sigmoid(gate)
    hidden = (gate * sigma * up).astype(jnp.bfloat16)
    up_term = (hidden_grad * gate * sigma).astype(jnp.bfloat16)
    gate_term = (hidden_grad * up * sigma * (1.0 + gate * (1.0 - sigma))).astype(jnp.bfloat16)
    return (hidden, gate_term, up_term)


def make_per_device(n_hid, n_wid):
    def per_device(inputs, gate_weight, up_weight, down_weight, out_grad):
        dw = inputs.shape[1]
        ff = gate_weight.shape[1]
        both = lax.all_gather(jnp.concatenate([inputs, out_grad], 1), ("chip", "core"), axis=0, tiled=True)
        all_inputs, all_grads = both[:, :dw], both[:, dw:]
        tokens = all_inputs.shape[0]
        contract_last = (((1,), (1,)), ((), ()))
        gate_part = jnp.dot(all_inputs, gate_weight, preferred_element_type=jnp.float32)
        up_part = jnp.dot(all_inputs, up_weight, preferred_element_type=jnp.float32)
        grad_part = lax.dot_general(
            all_grads, down_weight, contract_last, preferred_element_type=jnp.float32
        )
        parts = jnp.concatenate([gate_part, up_part, grad_part], 1).astype(jnp.bfloat16)
        parts = lax.all_to_all(parts.reshape(n_wid, tokens // n_wid, 3 * ff), "wid", 0, 0, tiled=False)
        sums = jnp.sum(parts.astype(jnp.float32), 0)
        gate, up, hidden_grad = sums[:, :ff], sums[:, ff:2 * ff], sums[:, 2 * ff:]
        terms = jnp.concatenate(swiglu_terms(gate, up, hidden_grad), 1)
        terms = jnp.broadcast_to(terms[None], (n_wid,) + terms.shape)
        terms = lax.all_to_all(terms, "wid", 0, 0, tiled=False).reshape(tokens, 3 * ff)
        hidden, gate_term, up_term = terms[:, :ff], terms[:, ff:2 * ff], terms[:, 2 * ff:]
        total = lax.dot_general(
            gate_term, gate_weight, contract_last, preferred_element_type=jnp.float32
        ) + lax.dot_general(up_term, up_weight, contract_last, preferred_element_type=jnp.float32)
        total = total.reshape(n_hid // 2, 2, tokens // n_hid, dw)
        total = jnp.sum(lax.all_to_all(total, "core", 1, 1, tiled=False), 1)
        total = lax.all_to_all(total, "chip", 0, 0, tiled=False)
        input_grad = jnp.sum(total, 0).astype(jnp.bfloat16)
        contract_first = (((0,), (0,)), ((), ()))
        gate_grad = lax.dot_general(
            all_inputs, gate_term, contract_first, preferred_element_type=jnp.float32
        ).astype(jnp.bfloat16)
        up_grad = lax.dot_general(
            all_inputs, up_term, contract_first, preferred_element_type=jnp.float32
        ).astype(jnp.bfloat16)
        down_grad = lax.dot_general(
            hidden, all_grads, contract_first, preferred_element_type=jnp.float32
        ).astype(jnp.bfloat16)
        return (input_grad, gate_grad, up_grad, down_grad)

    return per_device


def solution(mesh):
    n_hid, n_wid = mesh.shape["hid"], mesh.shape["wid"]
    split = Mesh(mesh.devices.reshape(n_hid // 2, 2, n_wid), ("chip", "core", "wid"))
    hid = ("chip", "core")
    placed = (P(hid, "wid"), P("wid", hid), P("wid", hid), P(hid, "wid"), P(hid, "wid"))
    return jax.shard_map(
        make_per_device(n_hid, n_wid),
        mesh=split,
        in_specs=placed,
        out_specs=(P(hid, "wid"), P("wid", hid), P("wid", hid), P(hid, "wid")),
        check_vma=False,
    )
```

```python
import jax
import jax.numpy as jnp
from jax import lax
from jax.sharding import Mesh, PartitionSpec as P


def swiglu_terms(gate, up, hidden_grad):
    sigma = jax.nn.sigmoid(gate)
    hidden = (gate * sigma * up).astype(jnp.bfloat16)
    up_term = (hidden_grad * gate * sigma).astype(jnp.bfloat16)
    gate_term = (hidden_grad * up * sigma * (1.0 + gate * (1.0 - sigma))).astype(jnp.bfloat16)
    return (hidden, gate_term, up_term)


def make_per_device(n_hid, n_wid):
    def per_device(inputs, gate_weight, up_weight, down_weight, out_grad):
        dw = inputs.shape[1]
        ff = gate_weight.shape[1]
        both = lax.all_gather(jnp.concatenate([inputs, out_grad], 1), ("chip", "core"), axis=0, tiled=True)
        all_inputs, all_grads = both[:, :dw], both[:, dw:]
        tokens = all_inputs.shape[0]
        contract_last = (((1,), (1,)), ((), ()))
        gate_part = jnp.dot(all_inputs, gate_weight, preferred_element_type=jnp.float32)
        up_part = jnp.dot(all_inputs, up_weight, preferred_element_type=jnp.float32)
        grad_part = lax.dot_general(
            all_grads, down_weight, contract_last, preferred_element_type=jnp.float32
        )
        parts = jnp.concatenate([gate_part, up_part, grad_part], 1).astype(jnp.bfloat16)
        parts = lax.all_to_all(parts.reshape(n_wid, tokens // n_wid, 3 * ff), "wid", 0, 0, tiled=False)
        sums = jnp.sum(parts.astype(jnp.float32), 0)
        gate, up, hidden_grad = sums[:, :ff], sums[:, ff:2 * ff], sums[:, 2 * ff:]
        terms = jnp.concatenate(swiglu_terms(gate, up, hidden_grad), 1)
        terms = jnp.broadcast_to(terms[None], (n_wid,) + terms.shape)
        terms = lax.all_to_all(terms, "wid", 0, 0, tiled=False).reshape(tokens, 3 * ff)
        hidden, gate_term, up_term = terms[:, :ff], terms[:, ff:2 * ff], terms[:, 2 * ff:]
        total = lax.dot_general(
            gate_term, gate_weight, contract_last, preferred_element_type=jnp.float32
        ) + lax.dot_general(up_term, up_weight, contract_last, preferred_element_type=jnp.float32)
        total = total.reshape(n_hid // 2, 2, tokens // n_hid, dw)
        total = jnp.sum(lax.all_to_all(total, "core", 1, 1, tiled=False), 1)
        total = lax.all_to_all(total.astype(jnp.bfloat16), "chip", 0, 0, tiled=False)
        input_grad = jnp.sum(total.astype(jnp.float32), 0).astype(jnp.bfloat16)
        contract_first = (((0,), (0,)), ((), ()))
        gate_grad = lax.dot_general(
            all_inputs, gate_term, contract_first, preferred_element_type=jnp.float32
        ).astype(jnp.bfloat16)
        up_grad = lax.dot_general(
            all_inputs, up_term, contract_first, preferred_element_type=jnp.float32
        ).astype(jnp.bfloat16)
        down_grad = lax.dot_general(
            hidden, all_grads, contract_first, preferred_element_type=jnp.float32
        ).astype(jnp.bfloat16)
        return (input_grad, gate_grad, up_grad, down_grad)

    return per_device


def solution(mesh):
    n_hid, n_wid = mesh.shape["hid"], mesh.shape["wid"]
    split = Mesh(mesh.devices.reshape(n_hid // 2, 2, n_wid), ("chip", "core", "wid"))
    hid = ("chip", "core")
    placed = (P(hid, "wid"), P("wid", hid), P("wid", hid), P(hid, "wid"), P(hid, "wid"))
    return jax.shard_map(
        make_per_device(n_hid, n_wid),
        mesh=split,
        in_specs=placed,
        out_specs=(P(hid, "wid"), P("wid", hid), P("wid", hid), P(hid, "wid")),
        check_vma=False,
    )
```

```python
import jax
import jax.numpy as jnp
from jax import lax
from jax.sharding import Mesh, PartitionSpec as P

HID = ("chip", "core")


def swiglu_terms(gate, up, hidden_grad):
    sigma = jax.nn.sigmoid(gate)
    hidden = (gate * sigma * up).astype(jnp.bfloat16)
    up_term = (hidden_grad * gate * sigma).astype(jnp.bfloat16)
    gate_term = (hidden_grad * up * sigma * (1.0 + gate * (1.0 - sigma))).astype(jnp.bfloat16)
    return (hidden, gate_term, up_term)


def make_per_device(n_hid, n_wid, n_chunk):
    def per_device(inputs, gate_weight, up_weight, down_weight, out_grad):
        rows, dw = inputs.shape
        ff = gate_weight.shape[1]
        rc = rows // n_chunk
        contract_last = (((1,), (1,)), ((), ()))
        both = jnp.concatenate([inputs, out_grad], 1)
        gathered, sums = [], []
        for k in range(n_chunk):
            g = lax.all_gather(both[k * rc:(k + 1) * rc], HID, axis=0, tiled=True)
            gathered.append(g)
            g_in, g_og = g[:, :dw], g[:, dw:]
            parts = jnp.concatenate([
                jnp.dot(g_in, gate_weight, preferred_element_type=jnp.float32),
                jnp.dot(g_in, up_weight, preferred_element_type=jnp.float32),
                lax.dot_general(g_og, down_weight, contract_last, preferred_element_type=jnp.float32),
            ], 1).astype(jnp.bfloat16)
            parts = lax.all_to_all(parts.reshape(n_wid, -1, 3 * ff), "wid", 0, 0, tiled=False)
            sums.append(jnp.sum(parts.astype(jnp.float32), 0))
        sums = jnp.stack(sums)
        gate, up, hidden_grad = sums[..., :ff], sums[..., ff:2 * ff], sums[..., 2 * ff:]
        terms = jnp.concatenate(swiglu_terms(gate, up, hidden_grad), -1)
        terms = jnp.broadcast_to(terms[None], (n_wid,) + terms.shape)
        terms = lax.all_to_all(terms, "wid", 0, 0, tiled=False)
        terms = jnp.swapaxes(terms, 0, 1).reshape(-1, 3 * ff)
        hidden, gate_term, up_term = terms[:, :ff], terms[:, ff:2 * ff], terms[:, 2 * ff:]
        gathered = jnp.concatenate(gathered, 0)
        all_inputs, all_grads = gathered[:, :dw], gathered[:, dw:]
        total = lax.dot_general(
            gate_term, gate_weight, contract_last, preferred_element_type=jnp.float32
        ) + lax.dot_general(up_term, up_weight, contract_last, preferred_element_type=jnp.float32)
        total = total.reshape(n_chunk, n_hid // 2, 2, rc, dw)
        total = jnp.sum(lax.all_to_all(total, "core", 2, 2, tiled=False), 2)
        total = lax.all_to_all(total.astype(jnp.bfloat16), "chip", 1, 1, tiled=False)
        input_grad = jnp.sum(total.astype(jnp.float32), 1).reshape(rows, dw).astype(jnp.bfloat16)
        contract_first = (((0,), (0,)), ((), ()))
        gate_grad = lax.dot_general(
            all_inputs, gate_term, contract_first, preferred_element_type=jnp.float32
        ).astype(jnp.bfloat16)
        up_grad = lax.dot_general(
            all_inputs, up_term, contract_first, preferred_element_type=jnp.float32
        ).astype(jnp.bfloat16)
        down_grad = lax.dot_general(
            hidden, all_grads, contract_first, preferred_element_type=jnp.float32
        ).astype(jnp.bfloat16)
        return (input_grad, gate_grad, up_grad, down_grad)

    return per_device


def solution(mesh):
    n_hid, n_wid = mesh.shape["hid"], mesh.shape["wid"]
    split = Mesh(mesh.devices.reshape(n_hid // 2, 2, n_wid), ("chip", "core", "wid"))
    placed = (P(HID, "wid"), P("wid", HID), P("wid", HID), P(HID, "wid"), P(HID, "wid"))
    return jax.shard_map(
        make_per_device(n_hid, n_wid, 2),
        mesh=split,
        in_specs=placed,
        out_specs=(P(HID, "wid"), P("wid", HID), P("wid", HID), P(HID, "wid")),
        check_vma=False,
    )
```

```python
import jax
import jax.numpy as jnp
from jax import lax
from jax.sharding import Mesh, PartitionSpec as P


def swiglu_terms(gate, up, hidden_grad):
    sigma = jax.nn.sigmoid(gate)
    hidden = (gate * sigma * up).astype(jnp.bfloat16)
    up_term = (hidden_grad * gate * sigma).astype(jnp.bfloat16)
    gate_term = (hidden_grad * up * sigma * (1.0 + gate * (1.0 - sigma))).astype(jnp.bfloat16)
    return (hidden, gate_term, up_term)


def make_per_device(n_hid, n_wid):
    def per_device(inputs, gate_weight, up_weight, down_weight, out_grad):
        dw = inputs.shape[1]
        ff = gate_weight.shape[1]
        both = lax.all_gather(jnp.concatenate([inputs, out_grad], 1), ("chip", "core"), axis=0, tiled=True)
        all_inputs, all_grads = both[:, :dw], both[:, dw:]
        tokens = all_inputs.shape[0]
        contract_last = (((1,), (1,)), ((), ()))
        gate_part = jnp.dot(all_inputs, gate_weight, preferred_element_type=jnp.float32)
        up_part = jnp.dot(all_inputs, up_weight, preferred_element_type=jnp.float32)
        grad_part = lax.dot_general(
            all_grads, down_weight, contract_last, preferred_element_type=jnp.float32
        )
        parts = jnp.concatenate([gate_part, up_part, grad_part], 1).astype(jnp.bfloat16)
        parts = lax.all_to_all(parts.reshape(n_wid, tokens // n_wid, 3 * ff), "wid", 0, 0, tiled=False)
        sums = jnp.sum(parts.astype(jnp.float32), 0)
        gate, up, hidden_grad = sums[:, :ff], sums[:, ff:2 * ff], sums[:, 2 * ff:]
        hidden, gate_term, up_term = swiglu_terms(gate, up, hidden_grad)
        hidden = lax.all_gather(hidden, "wid", axis=0, tiled=True)
        terms = jnp.concatenate([gate_term, up_term], 1)
        terms = jnp.broadcast_to(terms[None], (n_wid,) + terms.shape)
        terms = lax.all_to_all(terms, "wid", 0, 0, tiled=False).reshape(tokens, 2 * ff)
        gate_term, up_term = terms[:, :ff], terms[:, ff:]
        total = lax.dot_general(
            gate_term, gate_weight, contract_last, preferred_element_type=jnp.float32
        ) + lax.dot_general(up_term, up_weight, contract_last, preferred_element_type=jnp.float32)
        total = total.reshape(n_hid // 2, 2, tokens // n_hid, dw)
        total = jnp.sum(lax.all_to_all(total, "core", 1, 1, tiled=False), 1)
        total = lax.all_to_all(total.astype(jnp.bfloat16), "chip", 0, 0, tiled=False)
        input_grad = jnp.sum(total.astype(jnp.float32), 0).astype(jnp.bfloat16)
        contract_first = (((0,), (0,)), ((), ()))
        gate_grad = lax.dot_general(
            all_inputs, gate_term, contract_first, preferred_element_type=jnp.float32
        ).astype(jnp.bfloat16)
        up_grad = lax.dot_general(
            all_inputs, up_term, contract_first, preferred_element_type=jnp.float32
        ).astype(jnp.bfloat16)
        down_grad = lax.dot_general(
            hidden, all_grads, contract_first, preferred_element_type=jnp.float32
        ).astype(jnp.bfloat16)
        return (input_grad, gate_grad, up_grad, down_grad)

    return per_device


def solution(mesh):
    n_hid, n_wid = mesh.shape["hid"], mesh.shape["wid"]
    split = Mesh(mesh.devices.reshape(n_hid // 2, 2, n_wid), ("chip", "core", "wid"))
    hid = ("chip", "core")
    placed = (P(hid, "wid"), P("wid", hid), P("wid", hid), P(hid, "wid"), P(hid, "wid"))
    return jax.shard_map(
        make_per_device(n_hid, n_wid),
        mesh=split,
        in_specs=placed,
        out_specs=(P(hid, "wid"), P("wid", hid), P("wid", hid), P(hid, "wid")),
        check_vma=False,
    )
```

```python
import jax
import jax.numpy as jnp
from jax import lax
from jax.sharding import Mesh, PartitionSpec as P


def swiglu_terms(gate, up, hidden_grad):
    sigma = jax.nn.sigmoid(gate)
    hidden = (gate * sigma * up).astype(jnp.bfloat16)
    up_term = (hidden_grad * gate * sigma).astype(jnp.bfloat16)
    gate_term = (hidden_grad * up * sigma * (1.0 + gate * (1.0 - sigma))).astype(jnp.bfloat16)
    return (hidden, gate_term, up_term)


def make_per_device(n_hid, n_wid):
    def per_device(inputs, gate_weight, up_weight, down_weight, out_grad):
        dw = inputs.shape[1]
        ff = gate_weight.shape[1]
        both = lax.all_gather(jnp.concatenate([inputs, out_grad], 1), ("chip", "core"), axis=0, tiled=True)
        all_inputs, all_grads = both[:, :dw], both[:, dw:]
        tokens = all_inputs.shape[0]
        contract_last = (((1,), (1,)), ((), ()))
        gate_part = jnp.dot(all_inputs, gate_weight, preferred_element_type=jnp.float32)
        up_part = jnp.dot(all_inputs, up_weight, preferred_element_type=jnp.float32)
        grad_part = lax.dot_general(
            all_grads, down_weight, contract_last, preferred_element_type=jnp.float32
        )
        hidden_grad = lax.psum_scatter(
            grad_part.astype(jnp.bfloat16), "wid", scatter_dimension=0, tiled=True
        ).astype(jnp.float32)
        parts = jnp.concatenate([gate_part, up_part], 1).astype(jnp.bfloat16)
        parts = lax.all_to_all(parts.reshape(n_wid, tokens // n_wid, 2 * ff), "wid", 0, 0, tiled=False)
        sums = jnp.sum(parts.astype(jnp.float32), 0)
        gate, up = sums[:, :ff], sums[:, ff:]
        hidden, gate_term, up_term = swiglu_terms(gate, up, hidden_grad)
        hidden = lax.all_gather(hidden, "wid", axis=0, tiled=True)
        terms = jnp.concatenate([gate_term, up_term], 1)
        terms = jnp.broadcast_to(terms[None], (n_wid,) + terms.shape)
        terms = lax.all_to_all(terms, "wid", 0, 0, tiled=False).reshape(tokens, 2 * ff)
        gate_term, up_term = terms[:, :ff], terms[:, ff:]
        total = lax.dot_general(
            gate_term, gate_weight, contract_last, preferred_element_type=jnp.float32
        ) + lax.dot_general(up_term, up_weight, contract_last, preferred_element_type=jnp.float32)
        total = total.reshape(n_hid // 2, 2, tokens // n_hid, dw)
        total = jnp.sum(lax.all_to_all(total, "core", 1, 1, tiled=False), 1)
        total = lax.all_to_all(total.astype(jnp.bfloat16), "chip", 0, 0, tiled=False)
        input_grad = jnp.sum(total.astype(jnp.float32), 0).astype(jnp.bfloat16)
        contract_first = (((0,), (0,)), ((), ()))
        gate_grad = lax.dot_general(
            all_inputs, gate_term, contract_first, preferred_element_type=jnp.float32
        ).astype(jnp.bfloat16)
        up_grad = lax.dot_general(
            all_inputs, up_term, contract_first, preferred_element_type=jnp.float32
        ).astype(jnp.bfloat16)
        down_grad = lax.dot_general(
            hidden, all_grads, contract_first, preferred_element_type=jnp.float32
        ).astype(jnp.bfloat16)
        return (input_grad, gate_grad, up_grad, down_grad)

    return per_device


def solution(mesh):
    n_hid, n_wid = mesh.shape["hid"], mesh.shape["wid"]
    split = Mesh(mesh.devices.reshape(n_hid // 2, 2, n_wid), ("chip", "core", "wid"))
    hid = ("chip", "core")
    placed = (P(hid, "wid"), P("wid", hid), P("wid", hid), P(hid, "wid"), P(hid, "wid"))
    return jax.shard_map(
        make_per_device(n_hid, n_wid),
        mesh=split,
        in_specs=placed,
        out_specs=(P(hid, "wid"), P("wid", hid), P("wid", hid), P(hid, "wid")),
        check_vma=False,
    )
```

```python
import jax
import jax.numpy as jnp
from jax import lax
from jax.sharding import Mesh, PartitionSpec as P


def swiglu_terms(gate, up, hidden_grad):
    sigma = jax.nn.sigmoid(gate)
    hidden = (gate * sigma * up).astype(jnp.bfloat16)
    up_term = (hidden_grad * gate * sigma).astype(jnp.bfloat16)
    gate_term = (hidden_grad * up * sigma * (1.0 + gate * (1.0 - sigma))).astype(jnp.bfloat16)
    return (hidden, gate_term, up_term)


def make_per_device(n_hid, n_wid):
    def per_device(inputs, gate_weight, up_weight, down_weight, out_grad):
        dw = inputs.shape[1]
        ff = gate_weight.shape[1]
        both = lax.all_gather(jnp.concatenate([inputs, out_grad], 1), ("chip", "core"), axis=0, tiled=True)
        all_inputs, all_grads = both[:, :dw], both[:, dw:]
        tokens = all_inputs.shape[0]
        contract_last = (((1,), (1,)), ((), ()))
        gate_part = jnp.dot(all_inputs, gate_weight, preferred_element_type=jnp.float32)
        up_part = jnp.dot(all_inputs, up_weight, preferred_element_type=jnp.float32)
        grad_part = lax.dot_general(
            all_grads, down_weight, contract_last, preferred_element_type=jnp.float32
        )
        parts = jnp.concatenate([gate_part, up_part, grad_part], 1).astype(jnp.bfloat16)
        parts = lax.all_to_all(parts.reshape(n_wid, tokens // n_wid, 3 * ff), "wid", 0, 0, tiled=False)
        sums = jnp.sum(parts.astype(jnp.float32), 0)
        gate, up, hidden_grad = sums[:, :ff], sums[:, ff:2 * ff], sums[:, 2 * ff:]
        hidden, gate_term, up_term = swiglu_terms(gate, up, hidden_grad)
        hidden = lax.all_gather(hidden, "wid", axis=0, tiled=True)
        terms = jnp.concatenate([gate_term, up_term], 1)
        terms = jnp.broadcast_to(terms[None], (n_wid,) + terms.shape)
        terms = lax.all_to_all(terms, "wid", 0, 0, tiled=False).reshape(tokens, 2 * ff)
        gate_term, up_term = terms[:, :ff], terms[:, ff:]
        total = lax.dot_general(
            gate_term, gate_weight, contract_last, preferred_element_type=jnp.float32
        ) + lax.dot_general(up_term, up_weight, contract_last, preferred_element_type=jnp.float32)
        total = total.reshape(n_hid // 2, 2, tokens // n_hid, dw)
        total = lax.all_to_all(total.astype(jnp.bfloat16), "core", 1, 1, tiled=False)
        total = jnp.sum(total.astype(jnp.float32), 1)
        total = lax.all_to_all(total.astype(jnp.bfloat16), "chip", 0, 0, tiled=False)
        input_grad = jnp.sum(total.astype(jnp.float32), 0).astype(jnp.bfloat16)
        contract_first = (((0,), (0,)), ((), ()))
        gate_grad = lax.dot_general(
            all_inputs, gate_term, contract_first, preferred_element_type=jnp.float32
        ).astype(jnp.bfloat16)
        up_grad = lax.dot_general(
            all_inputs, up_term, contract_first, preferred_element_type=jnp.float32
        ).astype(jnp.bfloat16)
        down_grad = lax.dot_general(
            hidden, all_grads, contract_first, preferred_element_type=jnp.float32
        ).astype(jnp.bfloat16)
        return (input_grad, gate_grad, up_grad, down_grad)

    return per_device


def solution(mesh):
    n_hid, n_wid = mesh.shape["hid"], mesh.shape["wid"]
    split = Mesh(mesh.devices.reshape(n_hid // 2, 2, n_wid), ("chip", "core", "wid"))
    hid = ("chip", "core")
    placed = (P(hid, "wid"), P("wid", hid), P("wid", hid), P(hid, "wid"), P(hid, "wid"))
    return jax.shard_map(
        make_per_device(n_hid, n_wid),
        mesh=split,
        in_specs=placed,
        out_specs=(P(hid, "wid"), P("wid", hid), P("wid", hid), P(hid, "wid")),
        check_vma=False,
    )
```

```python
import jax
import jax.numpy as jnp
from jax import lax
from jax.sharding import Mesh, PartitionSpec as P


def swiglu_terms(gate, up, hidden_grad):
    sigma = jax.nn.sigmoid(gate)
    hidden = (gate * sigma * up).astype(jnp.bfloat16)
    up_term = (hidden_grad * gate * sigma).astype(jnp.bfloat16)
    gate_term = (hidden_grad * up * sigma * (1.0 + gate * (1.0 - sigma))).astype(jnp.bfloat16)
    return (hidden, gate_term, up_term)


def make_per_device(n_hid, n_wid):
    def per_device(inputs, gate_weight, up_weight, down_weight, out_grad):
        dw = inputs.shape[1]
        ff = gate_weight.shape[1]
        both = lax.all_gather(jnp.concatenate([inputs, out_grad], 1), ("chip", "core"), axis=0, tiled=True)
        all_inputs, all_grads = both[:, :dw], both[:, dw:]
        tokens = all_inputs.shape[0]
        contract_last = (((1,), (1,)), ((), ()))
        gate_part = jnp.dot(all_inputs, gate_weight, preferred_element_type=jnp.float32)
        up_part = jnp.dot(all_inputs, up_weight, preferred_element_type=jnp.float32)
        grad_part = lax.dot_general(
            all_grads, down_weight, contract_last, preferred_element_type=jnp.float32
        )
        parts = jnp.concatenate([gate_part, up_part, grad_part], 1).astype(jnp.bfloat16)
        parts = lax.all_to_all(parts.reshape(n_wid, tokens // n_wid, 3 * ff), "wid", 0, 0, tiled=False)
        sums = jnp.sum(parts.astype(jnp.float32), 0)
        gate, up, hidden_grad = sums[:, :ff], sums[:, ff:2 * ff], sums[:, 2 * ff:]
        hidden, gate_term, up_term = swiglu_terms(gate, up, hidden_grad)
        hidden = lax.all_gather(hidden, "wid", axis=0, tiled=True)
        terms = jnp.concatenate([gate_term, up_term], 1)
        terms = jnp.broadcast_to(terms[None], (n_wid,) + terms.shape)
        terms = lax.all_to_all(terms, "wid", 0, 0, tiled=False).reshape(tokens, 2 * ff)
        gate_term, up_term = terms[:, :ff], terms[:, ff:]
        core = lax.axis_index("core")
        by_core = (n_hid // 2, 2, tokens // n_hid, ff)

        def rows_of(which):
            g = lax.dynamic_index_in_dim(gate_term.reshape(by_core), which, 1, keepdims=False)
            u = lax.dynamic_index_in_dim(up_term.reshape(by_core), which, 1, keepdims=False)
            return lax.dot_general(
                g.reshape(-1, ff), gate_weight, contract_last, preferred_element_type=jnp.float32
            ) + lax.dot_general(u.reshape(-1, ff), up_weight, contract_last, preferred_element_type=jnp.float32)

        sent = lax.ppermute(rows_of(1 - core).astype(jnp.bfloat16), "core", [(0, 1), (1, 0)])
        total = rows_of(core) + sent.astype(jnp.float32)
        total = total.reshape(n_hid // 2, tokens // n_hid, dw)
        total = lax.all_to_all(total.astype(jnp.bfloat16), "chip", 0, 0, tiled=False)
        input_grad = jnp.sum(total.astype(jnp.float32), 0).astype(jnp.bfloat16)
        contract_first = (((0,), (0,)), ((), ()))
        gate_grad = lax.dot_general(
            all_inputs, gate_term, contract_first, preferred_element_type=jnp.float32
        ).astype(jnp.bfloat16)
        up_grad = lax.dot_general(
            all_inputs, up_term, contract_first, preferred_element_type=jnp.float32
        ).astype(jnp.bfloat16)
        down_grad = lax.dot_general(
            hidden, all_grads, contract_first, preferred_element_type=jnp.float32
        ).astype(jnp.bfloat16)
        return (input_grad, gate_grad, up_grad, down_grad)

    return per_device


def solution(mesh):
    n_hid, n_wid = mesh.shape["hid"], mesh.shape["wid"]
    split = Mesh(mesh.devices.reshape(n_hid // 2, 2, n_wid), ("chip", "core", "wid"))
    hid = ("chip", "core")
    placed = (P(hid, "wid"), P("wid", hid), P("wid", hid), P(hid, "wid"), P(hid, "wid"))
    return jax.shard_map(
        make_per_device(n_hid, n_wid),
        mesh=split,
        in_specs=placed,
        out_specs=(P(hid, "wid"), P("wid", hid), P("wid", hid), P(hid, "wid")),
        check_vma=False,
    )
```
